256 devices in a mesh: expert: 16 (over z, core), fsdp: 16 (over x, y).
Axes of the slice: x: 4, y: 4, z: 8, core: 2. Of those that a mesh axis runs over, the one named last changes fastest.
Arguments:
- tokens: bfloat16 [32768, 2048], P(('expert', 'fsdp')), may hold values from -6 to 6
- expert_ids: int32 [32768, 4], P(('expert', 'fsdp')), may hold values from 0 to 15, all different within a row; in each aligned block of 128 rows (0 to 127, 128 to 255, ...) at most 36 rows name the same one
- route_probs: float32 [32768, 4], P(('expert', 'fsdp')), may hold values from 0.1 to 1
- gate_weight: bfloat16 [16, 2048, 704], P('expert', 'fsdp'), may hold values from -0.125 to 0.125
- up_weight: bfloat16 [16, 2048, 704], P('expert', 'fsdp'), may hold values from -0.125 to 0.125
- down_weight: bfloat16 [16, 704, 2048], P('expert', None, 'fsdp'), may hold values from -0.21875 to 0.21875
- cotangent: bfloat16 [32768, 2048], P(('expert', 'fsdp')), may hold values from -0.59765625 to 0.59765625
Outputs:
- mixed: bfloat16 [32768, 2048], P(('expert', 'fsdp'))
- grad_probs: float32 [32768, 4], P(('expert', 'fsdp'))
- grad_tokens: bfloat16 [32768, 2048], P(('expert', 'fsdp'))
- grad_gate: bfloat16 [16, 2048, 704], P('expert', 'fsdp')
- grad_up: bfloat16 [16, 2048, 704], P('expert', 'fsdp')
- grad_down: bfloat16 [16, 704, 2048], P('expert', None, 'fsdp')
The draws below stay inside these ranges and needn't reach their ends.
Inputs may be any that keep to these rules, and one draw needn't show every extreme that they name: `expert_ids`: each token names 4 different experts; among the 128 tokens of one device no expert is named more than 36 times.
All inputs are finite; a program needn't handle non-finite values.
Results may differ from the reference program's by a relative error of at most 0.014.
Values may be sent and summed in bfloat16 or wider, within the bound.
No kernel may reach another device: no remote copies, remote signals or barrier semaphores. Data moves between devices by JAX's collectives and lax.ppermute only.
A program may use at most 128 MiB of HBM per device.

```python
import math
import jax
import jax.numpy as jnp
import numpy as np
from jax import lax

D = 2048
FFW = 704
TOP = 4
TOK_DEV = 128
EXPERTS = 16
CAP = 36
TOKENS = 32768
N_EXPERT = 16
N_FSDP = 16


def shard_levels(own_key, dims, pieces, smallest, largest):
    loudness, own = 1.0, jax.random.fold_in(own_key, 6)
    for axis_at, blocks in pieces:
        draws = jnp.exp(jax.random.uniform(jax.random.fold_in(own, axis_at), (blocks,), jnp.float32, smallest / len(pieces), largest / len(pieces)))
        loudness = loudness * jnp.repeat(draws, dims[axis_at] // blocks).reshape([-1 if axis == axis_at else 1 for axis in range(len(dims))])
    return loudness


def assign_block(own_key, own, number, rows, count, top, reach, skew):
    order = jax.random.permutation(own_key, count)
    packed, common = load_shares(count, rows * top, reach, skew, True), load_shares(count, rows * top, reach, skew, False)
    places = jnp.arange(count)

    def named(lengths, rotation):
        used = int((lengths > 0).sum())
        fixed = max(1, used // 4)
        passed = fixed + (places - fixed + rotation * (used - fixed)) % max(1, count - fixed)
        return jnp.zeros((count,), jnp.int32).at[order[jnp.where(places < fixed, places, passed)]].set(jnp.asarray(lengths, jnp.int32))

    lengths = jnp.where(number % 4 == 0, named(packed, number // 4), named(common, number - number // 4 - 1))
    mixed = jax.random.permutation(jax.random.fold_in(own, 3), count)
    source_of, sink = mixed[0:count // 2 * 2:2], mixed[1:count // 2 * 2:2]
    margin = jnp.minimum(lengths[source_of] - 1, reach - lengths[sink]) // 2
    margin = jnp.where((source_of == order[0]) | (sink == order[0]) | (lengths[sink] == 0), 0, jnp.maximum(margin, 0))
    passed = jax.random.randint(jax.random.fold_in(own, 4), (count // 2,), 0, 1 << 20) % (margin + 1)
    lengths = lengths.at[source_of].add(-passed).at[sink].add(passed)
    labels = jnp.searchsorted(jnp.cumsum(lengths), jnp.arange(rows * top), side="right").astype(jnp.int32)
    listing = labels.reshape(top, rows).T
    listing = listing[jax.random.permutation(jax.random.fold_in(own, 1), rows)]
    rotation = jax.random.randint(jax.random.fold_in(own, 2), (rows, 1), 0, top)
    return jnp.take_along_axis(listing, (jnp.arange(top)[None, :] + rotation) % top, axis=1)


def load_shares(count, total, limit, skew, full):
    loads = [(1 << 20) // math.isqrt(standing ** skew) + 1 for standing in range(1, count + 1)]
    largest = limit if full else min(limit, max(-(-total // count), total * loads[0] // sum(loads)))
    least = 1 if total - largest >= count - 1 else 0
    holding, rest = [largest] + [least] * (count - 1), total - largest - least * (count - 1)
    while rest > 0:
        movable = [i for i in range(1, count) if holding[i] < largest] or [i for i in range(1, count) if holding[i] < limit]
        mass, remaining = sum([loads[i] for i in movable]), rest
        for i in movable:
            extra = min(limit - holding[i], max(1, remaining * loads[i] // mass), rest)
            holding[i] = holding[i] + extra
            rest = rest - extra
    return np.array(holding)


def centred(own_key, shape, width, limit, pieces=(), kind=jnp.bfloat16):
    values = width * jax.random.normal(own_key, shape, jnp.float32)
    if pieces:
        values = values * shard_levels(own_key, shape, pieces, -0.22, 0.18)
    return jnp.clip(values, -limit, limit).astype(kind)


def setup_inputs(seed: int = 0) -> dict:
    arg_keys = jax.random.split(jax.random.key(seed), 8)
    tokens = centred(arg_keys[0], (TOKENS, D), 1.0, 6.0, ((0, 256),))
    expert_ids_keys = jax.random.split(jax.random.fold_in(arg_keys[1], 1), TOKENS // TOK_DEV)
    expert_ids_turns = jax.random.permutation(jax.random.fold_in(arg_keys[1], 3), TOKENS // TOK_DEV)
    expert_ids = jax.vmap(lambda own, number: assign_block(jax.random.fold_in(arg_keys[1], 2), own, number, TOK_DEV, EXPERTS, TOP, CAP, 2))(expert_ids_keys, expert_ids_turns).reshape((TOKENS, TOP))
    route_probs = jnp.clip(0.1 + 0.9 * jax.random.uniform(arg_keys[2], (TOKENS, TOP), jnp.float32) ** shard_levels(arg_keys[2], (TOKENS, TOP), ((0, 256),), -0.2, 0.2), 0.1, 1.0)
    gate_weight = centred(arg_keys[3], (EXPERTS, D, FFW), D ** -0.5, 0.125, ((0, 16), (1, 16)))
    up_weight = centred(arg_keys[4], (EXPERTS, D, FFW), D ** -0.5, 0.125, ((0, 16), (1, 16)))
    down_weight = centred(arg_keys[5], (EXPERTS, FFW, D), FFW ** -0.5, 0.21875, ((0, 16), (2, 16)))
    cotangent = centred(arg_keys[6], (TOKENS, D), 0.1, 0.59765625, ((0, 256),))
    return dict(tokens=tokens, expert_ids=expert_ids, route_probs=route_probs, gate_weight=gate_weight, up_weight=up_weight, down_weight=down_weight, cotangent=cotangent)


def placing(id_rows):
    flat_ids = id_rows.reshape(-1)
    onehot = (flat_ids[:, None] == jnp.arange(EXPERTS, dtype=jnp.int32)[None, :]).astype(jnp.int32)
    before = jnp.cumsum(onehot, axis=0) - onehot
    slot_index = jnp.sum(before * onehot, axis=1)
    target = flat_ids * CAP + slot_index
    dispatch = (jnp.arange(EXPERTS * CAP, dtype=jnp.int32)[:, None] == target[None, :]).astype(jnp.bfloat16)
    return dispatch, jnp.sum(onehot, axis=0)


def expert_forward(routed, live_mask, w_gate, w_up, w_down):
    gate_pre = jnp.dot(routed, w_gate, preferred_element_type=jnp.float32)
    up_pre = jnp.dot(routed, w_up, preferred_element_type=jnp.float32)
    hidden = (jax.nn.silu(gate_pre) * up_pre * live_mask[:, None]).astype(jnp.bfloat16)
    expert_out = jnp.dot(hidden, w_down, preferred_element_type=jnp.float32).astype(jnp.bfloat16)
    return gate_pre, up_pre, hidden, expert_out


def expert_backward(routed, grad_rows, gate_pre, up_pre, hidden, w_gate, w_up, w_down):
    grad_hidden = jnp.dot(grad_rows, w_down.T, preferred_element_type=jnp.float32)
    logistic = jax.nn.sigmoid(gate_pre)
    activated = gate_pre * logistic
    slope = logistic * (1.0 + gate_pre * (1.0 - logistic))
    grad_gate_pre = (grad_hidden * up_pre * slope).astype(jnp.bfloat16)
    grad_up_pre = (grad_hidden * activated).astype(jnp.bfloat16)
    row_grad = (jnp.dot(grad_gate_pre, w_gate.T, preferred_element_type=jnp.float32)
                + jnp.dot(grad_up_pre, w_up.T, preferred_element_type=jnp.float32)).astype(jnp.bfloat16)
    term_gate = jnp.dot(routed.T, grad_gate_pre, preferred_element_type=jnp.float32)
    term_up = jnp.dot(routed.T, grad_up_pre, preferred_element_type=jnp.float32)
    term_down = jnp.dot(hidden.T, grad_rows, preferred_element_type=jnp.float32)
    return row_grad, term_gate, term_up, term_down


def to_experts(array):
    moved = array.reshape(N_EXPERT, N_FSDP, EXPERTS, CAP, D)
    return jnp.transpose(moved, (2, 1, 0, 3, 4)).reshape(EXPERTS, N_FSDP, N_EXPERT * CAP, D)


def to_sources(array):
    moved = array.reshape(EXPERTS, N_FSDP, N_EXPERT, CAP, D)
    return jnp.transpose(moved, (2, 1, 0, 3, 4)).reshape(N_EXPERT * N_FSDP, EXPERTS * CAP, D)


def spread(pair):
    return jnp.dot(pair[0], pair[1], preferred_element_type=jnp.float32).astype(jnp.bfloat16)


def collect(pair):
    return jnp.dot(pair[0].T, pair[1], preferred_element_type=jnp.float32)


def reference(tokens, expert_ids, route_probs, gate_weight, up_weight, down_weight, cotangent):
    device_count = N_EXPERT * N_FSDP
    slot_count = EXPERTS * CAP
    token_rows = tokens.reshape(device_count, TOK_DEV, D)
    dispatch, counts = jax.vmap(placing)(expert_ids.reshape(device_count, TOK_DEV, TOP))
    dispatch_tok = dispatch.reshape(device_count, slot_count, TOK_DEV, TOP).sum(axis=3)
    arrived = to_experts(lax.map(spread, (dispatch_tok, token_rows)))
    arrived_counts = jnp.transpose(counts.reshape(N_EXPERT, N_FSDP, EXPERTS), (2, 1, 0))
    live_mask = (jnp.arange(CAP, dtype=jnp.int32)[None, None, None, :] < arrived_counts[..., None])
    live_mask = live_mask.astype(jnp.float32).reshape(EXPERTS, N_FSDP, N_EXPERT * CAP)

    def forward_expert(group):
        routed, masks, w_gate, w_up, w_down = group
        return lax.map(lambda member: expert_forward(member[0], member[1], w_gate, w_up, w_down), (routed, masks))

    gate_pre, up_pre, hidden, expert_out = lax.map(forward_expert, (arrived, live_mask, gate_weight, up_weight, down_weight))
    combined = lax.map(collect, (dispatch, to_sources(expert_out))).reshape(TOKENS, TOP, D)
    mixed = jnp.einsum("tk,tkd->td", route_probs, combined).astype(jnp.bfloat16)
    upstream = cotangent.astype(jnp.float32)
    grad_probs = jnp.einsum("td,tkd->tk", upstream, combined)
    grad_out = (route_probs[:, :, None] * upstream[:, None, :]).astype(jnp.bfloat16)
    grad_out = grad_out.reshape(device_count, TOK_DEV * TOP, D)
    arrived_grad = to_experts(lax.map(spread, (dispatch, grad_out)))

    def backward_expert(group):
        routed, grads, gates, ups, hiddens, w_gate, w_up, w_down = group
        zeros_in = jnp.zeros((D, FFW), jnp.float32)
        zeros_out = jnp.zeros((FFW, D), jnp.float32)

        def accumulate(sums, member):
            row_grad, term_gate, term_up, term_down = expert_backward(member[0], member[1], member[2], member[3], member[4], w_gate, w_up, w_down)
            rounded = lax.optimization_barrier((term_gate.astype(jnp.bfloat16), term_up.astype(jnp.bfloat16), term_down.astype(jnp.bfloat16)))
            new_sums = (sums[0] + rounded[0].astype(jnp.float32), sums[1] + rounded[1].astype(jnp.float32), sums[2] + rounded[2].astype(jnp.float32))
            return new_sums, row_grad

        sums, row_grads = lax.scan(accumulate, (zeros_in, zeros_in, zeros_out), (routed, grads, gates, ups, hiddens))
        return sums[0].astype(jnp.bfloat16), sums[1].astype(jnp.bfloat16), sums[2].astype(jnp.bfloat16), row_grads

    grad_gate, grad_up, grad_down, row_grads = lax.map(backward_expert, (arrived, arrived_grad, gate_pre, up_pre, hidden, gate_weight, up_weight, down_weight))
    grad_rows = lax.map(collect, (dispatch, to_sources(row_grads))).reshape(TOKENS, TOP, D)
    grad_tokens = grad_rows.sum(axis=1).astype(jnp.bfloat16)
    return (mixed, grad_probs, grad_tokens, grad_gate, grad_up, grad_down)
```

```python
import jax
import jax.numpy as jnp
from jax import lax
from jax.sharding import PartitionSpec as P


def routing(id_rows, experts, capacity):
    flat_ids = id_rows.reshape(-1)
    onehot = (flat_ids[:, None] == jnp.arange(experts, dtype=jnp.int32)[None, :]).astype(jnp.int32)
    before = jnp.cumsum(onehot, axis=0) - onehot
    slot_index = jnp.sum(before * onehot, axis=1)
    target = flat_ids * capacity + slot_index
    slots = experts * capacity
    dispatch = jnp.arange(slots, dtype=jnp.int32)[:, None] == target[None, :]
    return (dispatch, jnp.sum(onehot, axis=0))


def expert_forward(routed, live_mask, w_gate, w_up, w_down_blocks):
    gate_pre = jnp.dot(routed, w_gate, preferred_element_type=jnp.float32)
    up_pre = jnp.dot(routed, w_up, preferred_element_type=jnp.float32)
    hidden = (jax.nn.silu(gate_pre) * up_pre * live_mask[:, None]).astype(jnp.bfloat16)
    expert_out = jnp.einsum(
        "sf,jfd->sjd", hidden, w_down_blocks, preferred_element_type=jnp.float32
    ).astype(jnp.bfloat16)
    return (gate_pre, up_pre, hidden, expert_out.reshape(hidden.shape[0], -1))


def expert_backward(routed, grad_rows, gate_pre, up_pre, hidden, w_gate, w_up, w_down_blocks):
    grad_blocks = grad_rows.reshape(grad_rows.shape[0], w_down_blocks.shape[0], -1)
    grad_hidden = jnp.einsum(
        "sjd,jfd->sf", grad_blocks, w_down_blocks, preferred_element_type=jnp.float32
    )
    logistic = jax.nn.sigmoid(gate_pre)
    activated = gate_pre * logistic
    slope = logistic * (1.0 + gate_pre * (1.0 - logistic))
    grad_gate_pre = (grad_hidden * up_pre * slope).astype(jnp.bfloat16)
    grad_up_pre = (grad_hidden * activated).astype(jnp.bfloat16)
    row_grad = (
        jnp.dot(grad_gate_pre, w_gate.T, preferred_element_type=jnp.float32)
        + jnp.dot(grad_up_pre, w_up.T, preferred_element_type=jnp.float32)
    ).astype(jnp.bfloat16)
    term_gate = jnp.dot(routed.T, grad_gate_pre, preferred_element_type=jnp.float32)
    term_up = jnp.dot(routed.T, grad_up_pre, preferred_element_type=jnp.float32)
    term_down_t = jnp.dot(grad_rows.T, hidden, preferred_element_type=jnp.float32)
    return (row_grad, term_gate, term_up, term_down_t)


def gather_fsdp(shard, n_fsdp):
    me = lax.axis_index("fsdp")
    full = jnp.zeros((n_fsdp,) + shard.shape, shard.dtype)
    full = lax.dynamic_update_index_in_dim(full, shard, me, 0)
    for s in range(1, n_fsdp):
        pairs = [(i, (i + s) % n_fsdp) for i in range(n_fsdp)]
        got = lax.ppermute(shard, "fsdp", pairs)
        full = lax.dynamic_update_index_in_dim(full, got, (me - s) % n_fsdp, 0)
    return full


def scatter_sum_fsdp(term, n_fsdp):
    me = lax.axis_index("fsdp")
    blocks = term.astype(jnp.bfloat16).reshape((n_fsdp, term.shape[0] // n_fsdp) + term.shape[1:])
    total = lax.dynamic_index_in_dim(blocks, me, 0, keepdims=False).astype(jnp.float32)
    for s in range(1, n_fsdp):
        pairs = [(i, (i + s) % n_fsdp) for i in range(n_fsdp)]
        part = lax.dynamic_index_in_dim(blocks, (me + s) % n_fsdp, 0, keepdims=False)
        total = total + lax.ppermute(part, "fsdp", pairs).astype(jnp.float32)
    return total.astype(jnp.bfloat16)


def per_device(tokens, expert_ids, route_probs, gate_weight, up_weight, down_weight, cotangent):
    n_expert = lax.axis_size("expert")
    n_fsdp = lax.axis_size("fsdp")
    experts = n_expert * gate_weight.shape[0]
    tok_dev, choose = expert_ids.shape
    features = tokens.shape[1]
    capacity = tok_dev * choose * 9 // (experts * 8)
    slot_count = experts * capacity
    dispatch, counts = routing(expert_ids, experts, capacity)
    dispatch_pair = dispatch.astype(jnp.bfloat16)
    dispatch_tok = jnp.sum(dispatch.reshape(slot_count, tok_dev, choose), axis=2).astype(jnp.bfloat16)
    outgoing = jnp.dot(dispatch_tok, tokens, preferred_element_type=jnp.float32).astype(jnp.bfloat16)
    sent_counts = counts.astype(jnp.bfloat16).reshape(experts, 1)
    arrived = lax.all_to_all(
        outgoing.reshape(experts, capacity, features), "expert", split_axis=0, concat_axis=0, tiled=True
    )
    arrived_counts = lax.all_to_all(sent_counts, "expert", split_axis=0, concat_axis=0, tiled=True)
    upstream = cotangent.astype(jnp.float32)
    slot_probs = jnp.sum(
        jnp.where(dispatch, route_probs.reshape(1, tok_dev * choose), 0.0), axis=1
    )
    slot_cot = jnp.dot(dispatch_tok, cotangent, preferred_element_type=jnp.float32)
    outgoing_grad = (slot_probs[:, None] * slot_cot).astype(jnp.bfloat16)
    arrived_grad = lax.all_to_all(
        outgoing_grad.reshape(experts, capacity, features), "expert", split_axis=0, concat_axis=0, tiled=True
    )
    routed = arrived.reshape(slot_count, features)
    grad_rows = arrived_grad.reshape(slot_count, features)
    live_mask = jnp.arange(capacity, dtype=jnp.float32)[None, :] < arrived_counts.astype(jnp.float32)
    live_mask = live_mask.astype(jnp.float32).reshape(slot_count)
    w_gate = gather_fsdp(gate_weight[0], n_fsdp).reshape(features, -1)
    w_up = gather_fsdp(up_weight[0], n_fsdp).reshape(features, -1)
    w_down_blocks = gather_fsdp(down_weight[0], n_fsdp)
    gate_pre, up_pre, hidden, expert_out = expert_forward(routed, live_mask, w_gate, w_up, w_down_blocks)
    returned = lax.all_to_all(
        expert_out.reshape(n_expert, capacity, features), "expert", split_axis=0, concat_axis=0, tiled=True
    )
    row_grad, term_gate, term_up, term_down_t = expert_backward(
        routed, grad_rows, gate_pre, up_pre, hidden, w_gate, w_up, w_down_blocks
    )
    returned_grad = lax.all_to_all(
        row_grad.reshape(n_expert, capacity, features), "expert", split_axis=0, concat_axis=0, tiled=True
    )
    summed_gate = scatter_sum_fsdp(term_gate, n_fsdp)
    summed_up = scatter_sum_fsdp(term_up, n_fsdp)
    summed_down = scatter_sum_fsdp(term_down_t, n_fsdp).T
    combined = lax.dot_general(
        dispatch_pair,
        returned.reshape(slot_count, features),
        (((0,), (0,)), ((), ())),
        preferred_element_type=jnp.float32,
    ).reshape(tok_dev, choose, features)
    mixed = jnp.einsum("tk,tkd->td", route_probs, combined).astype(jnp.bfloat16)
    grad_probs = jnp.einsum("td,tkd->tk", upstream, combined)
    grad_tokens = lax.dot_general(
        dispatch_tok,
        returned_grad.reshape(slot_count, features),
        (((0,), (0,)), ((), ())),
        preferred_element_type=jnp.float32,
    ).astype(jnp.bfloat16)
    return (
        mixed,
        grad_probs,
        grad_tokens,
        summed_gate[None],
        summed_up[None],
        summed_down[None],
    )


def solution(mesh):
    return jax.shard_map(
        per_device,
        mesh=mesh,
        in_specs=(
            P(("expert", "fsdp"), None),
            P(("expert", "fsdp"), None),
            P(("expert", "fsdp"), None),
            P("expert", "fsdp", None),
            P("expert", "fsdp", None),
            P("expert", None, "fsdp"),
            P(("expert", "fsdp"), None),
        ),
        out_specs=(
            P(("expert", "fsdp"), None),
            P(("expert", "fsdp"), None),
            P(("expert", "fsdp"), None),
            P("expert", "fsdp", None),
            P("expert", "fsdp", None),
            P("expert", None, "fsdp"),
        ),
        check_vma=False,
    )
```

```python
import jax
import jax.numpy as jnp
from jax import lax
from jax.sharding import PartitionSpec as P


def routing(id_rows, experts, capacity):
    flat_ids = id_rows.reshape(-1)
    onehot = (flat_ids[:, None] == jnp.arange(experts, dtype=jnp.int32)[None, :]).astype(jnp.int32)
    before = jnp.cumsum(onehot, axis=0) - onehot
    slot_index = jnp.sum(before * onehot, axis=1)
    target = flat_ids * capacity + slot_index
    slots = experts * capacity
    dispatch = jnp.arange(slots, dtype=jnp.int32)[:, None] == target[None, :]
    return (dispatch, jnp.sum(onehot, axis=0))


def expert_forward(routed, live_mask, w_gate, w_up, w_down_blocks):
    gate_pre = jnp.dot(routed, w_gate, preferred_element_type=jnp.float32)
    up_pre = jnp.dot(routed, w_up, preferred_element_type=jnp.float32)
    hidden = (jax.nn.silu(gate_pre) * up_pre * live_mask[:, None]).astype(jnp.bfloat16)
    expert_out = jnp.einsum(
        "sf,jfd->sjd", hidden, w_down_blocks, preferred_element_type=jnp.float32
    ).astype(jnp.bfloat16)
    return (gate_pre, up_pre, hidden, expert_out.reshape(hidden.shape[0], -1))


def expert_backward(routed, grad_rows, gate_pre, up_pre, hidden, w_gate, w_up, w_down_blocks):
    grad_blocks = grad_rows.reshape(grad_rows.shape[0], w_down_blocks.shape[0], -1)
    grad_hidden = jnp.einsum(
        "sjd,jfd->sf", grad_blocks, w_down_blocks, preferred_element_type=jnp.float32
    )
    logistic = jax.nn.sigmoid(gate_pre)
    activated = gate_pre * logistic
    slope = logistic * (1.0 + gate_pre * (1.0 - logistic))
    grad_gate_pre = (grad_hidden * up_pre * slope).astype(jnp.bfloat16)
    grad_up_pre = (grad_hidden * activated).astype(jnp.bfloat16)
    row_grad = (
        jnp.dot(grad_gate_pre, w_gate.T, preferred_element_type=jnp.float32)
        + jnp.dot(grad_up_pre, w_up.T, preferred_element_type=jnp.float32)
    ).astype(jnp.bfloat16)
    term_gate = jnp.dot(routed.T, grad_gate_pre, preferred_element_type=jnp.float32)
    term_up = jnp.dot(routed.T, grad_up_pre, preferred_element_type=jnp.float32)
    term_down_t = jnp.dot(grad_rows.T, hidden, preferred_element_type=jnp.float32)
    return (row_grad, term_gate, term_up, term_down_t)


def gather_fsdp(shard, n_fsdp):
    copies = jnp.broadcast_to(shard[None], (n_fsdp,) + shard.shape)
    return lax.all_to_all(copies, "fsdp", split_axis=0, concat_axis=0, tiled=True)


def scatter_sum_fsdp(terms, n_fsdp):
    stacked = jnp.stack([t.astype(jnp.bfloat16) for t in terms], axis=0)
    count, rows = stacked.shape[0], stacked.shape[1] // n_fsdp
    blocks = stacked.reshape((count, n_fsdp, rows) + stacked.shape[2:]).swapaxes(0, 1)
    got = lax.all_to_all(blocks, "fsdp", split_axis=0, concat_axis=0, tiled=True)
    summed = jnp.sum(got.astype(jnp.float32), axis=0).astype(jnp.bfloat16)
    return [summed[i] for i in range(count)]


def per_device(tokens, expert_ids, route_probs, gate_weight, up_weight, down_weight, cotangent):
    n_expert = lax.axis_size("expert")
    n_fsdp = lax.axis_size("fsdp")
    experts = n_expert * gate_weight.shape[0]
    tok_dev, choose = expert_ids.shape
    features = tokens.shape[1]
    capacity = tok_dev * choose * 9 // (experts * 8)
    slot_count = experts * capacity
    dispatch, counts = routing(expert_ids, experts, capacity)
    dispatch_pair = dispatch.astype(jnp.bfloat16)
    dispatch_tok = jnp.sum(dispatch.reshape(slot_count, tok_dev, choose), axis=2).astype(jnp.bfloat16)
    outgoing = jnp.dot(dispatch_tok, tokens, preferred_element_type=jnp.float32).astype(jnp.bfloat16)
    sent_counts = counts.astype(jnp.bfloat16).reshape(experts, 1)
    arrived = lax.all_to_all(
        outgoing.reshape(experts, capacity, features), "expert", split_axis=0, concat_axis=0, tiled=True
    )
    arrived_counts = lax.all_to_all(sent_counts, "expert", split_axis=0, concat_axis=0, tiled=True)
    upstream = cotangent.astype(jnp.float32)
    slot_probs = jnp.sum(
        jnp.where(dispatch, route_probs.reshape(1, tok_dev * choose), 0.0), axis=1
    )
    slot_cot = jnp.dot(dispatch_tok, cotangent, preferred_element_type=jnp.float32)
    outgoing_grad = (slot_probs[:, None] * slot_cot).astype(jnp.bfloat16)
    w_gate = gather_fsdp(gate_weight[0], n_fsdp).reshape(features, -1)
    w_gate, outgoing_grad = lax.optimization_barrier((w_gate, outgoing_grad))
    arrived_grad = lax.all_to_all(
        outgoing_grad.reshape(experts, capacity, features), "expert", split_axis=0, concat_axis=0, tiled=True
    )
    routed = arrived.reshape(slot_count, features)
    grad_rows = arrived_grad.reshape(slot_count, features)
    live_mask = jnp.arange(capacity, dtype=jnp.float32)[None, :] < arrived_counts.astype(jnp.float32)
    live_mask = live_mask.astype(jnp.float32).reshape(slot_count)
    w_up = lax.all_gather(up_weight, "fsdp", axis=1, tiled=True)[0]
    w_down = lax.all_gather(down_weight, "fsdp", axis=2, tiled=True)[0]
    w_down_blocks = w_down.reshape(w_down.shape[0], n_fsdp, -1).swapaxes(0, 1)
    gate_pre, up_pre, hidden, expert_out = expert_forward(routed, live_mask, w_gate, w_up, w_down_blocks)
    returned = lax.all_to_all(
        expert_out.reshape(n_expert, capacity, features), "expert", split_axis=0, concat_axis=0, tiled=True
    )
    row_grad, term_gate, term_up, term_down_t = expert_backward(
        routed, grad_rows, gate_pre, up_pre, hidden, w_gate, w_up, w_down_blocks
    )
    returned_grad = lax.all_to_all(
        row_grad.reshape(n_expert, capacity, features), "expert", split_axis=0, concat_axis=0, tiled=True
    )
    summed_gate, summed_up = scatter_sum_fsdp([term_gate, term_up], n_fsdp)
    summed_down = lax.psum_scatter(
        term_down_t.T.astype(jnp.bfloat16), "fsdp", scatter_dimension=1, tiled=True
    )
    combined = lax.dot_general(
        dispatch_pair,
        returned.reshape(slot_count, features),
        (((0,), (0,)), ((), ())),
        preferred_element_type=jnp.float32,
    ).reshape(tok_dev, choose, features)
    mixed = jnp.einsum("tk,tkd->td", route_probs, combined).astype(jnp.bfloat16)
    grad_probs = jnp.einsum("td,tkd->tk", upstream, combined)
    grad_tokens = lax.dot_general(
        dispatch_tok,
        returned_grad.reshape(slot_count, features),
        (((0,), (0,)), ((), ())),
        preferred_element_type=jnp.float32,
    ).astype(jnp.bfloat16)
    return (
        mixed,
        grad_probs,
        grad_tokens,
        summed_gate[None],
        summed_up[None],
        summed_down[None],
    )


def solution(mesh):
    return jax.shard_map(
        per_device,
        mesh=mesh,
        in_specs=(
            P(("expert", "fsdp"), None),
            P(("expert", "fsdp"), None),
            P(("expert", "fsdp"), None),
            P("expert", "fsdp", None),
            P("expert", "fsdp", None),
            P("expert", None, "fsdp"),
            P(("expert", "fsdp"), None),
        ),
        out_specs=(
            P(("expert", "fsdp"), None),
            P(("expert", "fsdp"), None),
            P(("expert", "fsdp"), None),
            P("expert", "fsdp", None),
            P("expert", "fsdp", None),
            P("expert", None, "fsdp"),
        ),
        check_vma=False,
    )
```

```python
import jax
import jax.numpy as jnp
from jax import lax
from jax.sharding import PartitionSpec as P


def routing(id_rows, experts, capacity):
    flat_ids = id_rows.reshape(-1)
    onehot = (flat_ids[:, None] == jnp.arange(experts, dtype=jnp.int32)[None, :]).astype(jnp.int32)
    before = jnp.cumsum(onehot, axis=0) - onehot
    slot_index = jnp.sum(before * onehot, axis=1)
    target = flat_ids * capacity + slot_index
    slots = experts * capacity
    dispatch = jnp.arange(slots, dtype=jnp.int32)[:, None] == target[None, :]
    return (dispatch, jnp.sum(onehot, axis=0))


def expert_forward(routed, live_mask, w_gate, w_up, w_down_blocks):
    gate_pre = jnp.dot(routed, w_gate, preferred_element_type=jnp.float32)
    up_pre = jnp.dot(routed, w_up, preferred_element_type=jnp.float32)
    hidden = (jax.nn.silu(gate_pre) * up_pre * live_mask[:, None]).astype(jnp.bfloat16)
    expert_out = jnp.einsum(
        "sf,jfd->sjd", hidden, w_down_blocks, preferred_element_type=jnp.float32
    ).astype(jnp.bfloat16)
    return (gate_pre, up_pre, hidden, expert_out.reshape(hidden.shape[0], -1))


def expert_backward(routed, grad_rows, gate_pre, up_pre, hidden, w_gate, w_up, w_down_blocks):
    grad_blocks = grad_rows.reshape(grad_rows.shape[0], w_down_blocks.shape[0], -1)
    grad_hidden = jnp.einsum(
        "sjd,jfd->sf", grad_blocks, w_down_blocks, preferred_element_type=jnp.float32
    )
    logistic = jax.nn.sigmoid(gate_pre)
    activated = gate_pre * logistic
    slope = logistic * (1.0 + gate_pre * (1.0 - logistic))
    grad_gate_pre = (grad_hidden * up_pre * slope).astype(jnp.bfloat16)
    grad_up_pre = (grad_hidden * activated).astype(jnp.bfloat16)
    row_grad = (
        jnp.dot(grad_gate_pre, w_gate.T, preferred_element_type=jnp.float32)
        + jnp.dot(grad_up_pre, w_up.T, preferred_element_type=jnp.float32)
    ).astype(jnp.bfloat16)
    term_gate = jnp.dot(routed.T, grad_gate_pre, preferred_element_type=jnp.float32)
    term_up = jnp.dot(routed.T, grad_up_pre, preferred_element_type=jnp.float32)
    term_down_t = jnp.dot(grad_rows.T, hidden, preferred_element_type=jnp.float32)
    return (row_grad, term_gate, term_up, term_down_t)


def gather_fsdp(shard, n_fsdp):
    copies = jnp.broadcast_to(shard[None], (n_fsdp,) + shard.shape)
    return lax.all_to_all(copies, "fsdp", split_axis=0, concat_axis=0, tiled=True)


def scatter_sum_fsdp(terms, n_fsdp):
    stacked = jnp.stack([t.astype(jnp.bfloat16) for t in terms], axis=0)
    count, rows = stacked.shape[0], stacked.shape[1] // n_fsdp
    blocks = stacked.reshape((count, n_fsdp, rows) + stacked.shape[2:]).swapaxes(0, 1)
    got = lax.all_to_all(blocks, "fsdp", split_axis=0, concat_axis=0, tiled=True)
    summed = jnp.sum(got.astype(jnp.float32), axis=0).astype(jnp.bfloat16)
    return [summed[i] for i in range(count)]


def per_device(tokens, expert_ids, route_probs, gate_weight, up_weight, down_weight, cotangent):
    n_expert = lax.axis_size("expert")
    n_fsdp = lax.axis_size("fsdp")
    experts = n_expert * gate_weight.shape[0]
    tok_dev, choose = expert_ids.shape
    features = tokens.shape[1]
    capacity = tok_dev * choose * 9 // (experts * 8)
    slot_count = experts * capacity
    dispatch, counts = routing(expert_ids, experts, capacity)
    dispatch_pair = dispatch.astype(jnp.bfloat16)
    dispatch_tok = jnp.sum(dispatch.reshape(slot_count, tok_dev, choose), axis=2).astype(jnp.bfloat16)
    outgoing = jnp.dot(dispatch_tok, tokens, preferred_element_type=jnp.float32).astype(jnp.bfloat16)
    count_rows = jnp.zeros((experts, 1, features), jnp.bfloat16)
    count_rows = count_rows.at[:, 0, 0].set(counts.astype(jnp.bfloat16))
    payload = jnp.concatenate([outgoing.reshape(experts, capacity, features), count_rows], axis=1)
    arrived_all = lax.all_to_all(payload, "expert", split_axis=0, concat_axis=0, tiled=True)
    arrived = arrived_all[:, :capacity]
    arrived_counts = arrived_all[:, capacity, 0:1]
    upstream = cotangent.astype(jnp.float32)
    slot_probs = jnp.sum(
        jnp.where(dispatch, route_probs.reshape(1, tok_dev * choose), 0.0), axis=1
    )
    slot_cot = jnp.dot(dispatch_tok, cotangent, preferred_element_type=jnp.float32)
    outgoing_grad = (slot_probs[:, None] * slot_cot).astype(jnp.bfloat16)
    arrived_all, outgoing_grad = lax.optimization_barrier((arrived_all, outgoing_grad))
    arrived_grad = lax.all_to_all(
        outgoing_grad.reshape(experts, capacity, features), "expert", split_axis=0, concat_axis=0, tiled=True
    )
    routed = arrived.reshape(slot_count, features)
    grad_rows = arrived_grad.reshape(slot_count, features)
    live_mask = jnp.arange(capacity, dtype=jnp.float32)[None, :] < arrived_counts.astype(jnp.float32)
    live_mask = live_mask.astype(jnp.float32).reshape(slot_count)
    w_gate = lax.all_gather(gate_weight, "fsdp", axis=1, tiled=True)[0]
    w_up = lax.all_gather(up_weight, "fsdp", axis=1, tiled=True)[0]
    w_down = lax.all_gather(down_weight, "fsdp", axis=2, tiled=True)[0]
    w_down_blocks = w_down.reshape(w_down.shape[0], n_fsdp, -1).swapaxes(0, 1)
    gate_pre, up_pre, hidden, expert_out = expert_forward(routed, live_mask, w_gate, w_up, w_down_blocks)
    returned = lax.all_to_all(
        expert_out.reshape(n_expert, capacity, features), "expert", split_axis=0, concat_axis=0, tiled=True
    )
    row_grad, term_gate, term_up, term_down_t = expert_backward(
        routed, grad_rows, gate_pre, up_pre, hidden, w_gate, w_up, w_down_blocks
    )
    returned_grad = lax.all_to_all(
        row_grad.reshape(n_expert, capacity, features), "expert", split_axis=0, concat_axis=0, tiled=True
    )
    summed_gate = lax.psum_scatter(
        term_gate.astype(jnp.bfloat16), "fsdp", scatter_dimension=0, tiled=True
    )
    returned, term_up = lax.optimization_barrier((returned, term_up))
    (summed_up,) = scatter_sum_fsdp([term_up], n_fsdp)
    summed_down = lax.psum_scatter(
        term_down_t.T.astype(jnp.bfloat16), "fsdp", scatter_dimension=1, tiled=True
    )
    combined = lax.dot_general(
        dispatch_pair,
        returned.reshape(slot_count, features),
        (((0,), (0,)), ((), ())),
        preferred_element_type=jnp.float32,
    ).reshape(tok_dev, choose, features)
    mixed = jnp.einsum("tk,tkd->td", route_probs, combined).astype(jnp.bfloat16)
    grad_probs = jnp.einsum("td,tkd->tk", upstream, combined)
    grad_tokens = lax.dot_general(
        dispatch_tok,
        returned_grad.reshape(slot_count, features),
        (((0,), (0,)), ((), ())),
        preferred_element_type=jnp.float32,
    ).astype(jnp.bfloat16)
    return (
        mixed,
        grad_probs,
        grad_tokens,
        summed_gate[None],
        summed_up[None],
        summed_down[None],
    )


def solution(mesh):
    return jax.shard_map(
        per_device,
        mesh=mesh,
        in_specs=(
            P(("expert", "fsdp"), None),
            P(("expert", "fsdp"), None),
            P(("expert", "fsdp"), None),
            P("expert", "fsdp", None),
            P("expert", "fsdp", None),
            P("expert", None, "fsdp"),
            P(("expert", "fsdp"), None),
        ),
        out_specs=(
            P(("expert", "fsdp"), None),
            P(("expert", "fsdp"), None),
            P(("expert", "fsdp"), None),
            P("expert", "fsdp", None),
            P("expert", "fsdp", None),
            P("expert", None, "fsdp"),
        ),
        check_vma=False,
    )
```

```python
import jax
import jax.numpy as jnp
from jax import lax
from jax.sharding import PartitionSpec as P


def routing(id_rows, experts, capacity):
    flat_ids = id_rows.reshape(-1)
    onehot = (flat_ids[:, None] == jnp.arange(experts, dtype=jnp.int32)[None, :]).astype(jnp.int32)
    before = jnp.cumsum(onehot, axis=0) - onehot
    slot_index = jnp.sum(before * onehot, axis=1)
    target = flat_ids * capacity + slot_index
    slots = experts * capacity
    dispatch = jnp.arange(slots, dtype=jnp.int32)[:, None] == target[None, :]
    return (dispatch, jnp.sum(onehot, axis=0))


def expert_forward(routed, live_mask, w_gate, w_up, w_down_blocks):
    gate_pre = jnp.dot(routed, w_gate, preferred_element_type=jnp.float32)
    up_pre = jnp.dot(routed, w_up, preferred_element_type=jnp.float32)
    hidden = (jax.nn.silu(gate_pre) * up_pre * live_mask[:, None]).astype(jnp.bfloat16)
    expert_out = jnp.einsum(
        "sf,jfd->sjd", hidden, w_down_blocks, preferred_element_type=jnp.float32
    ).astype(jnp.bfloat16)
    return (gate_pre, up_pre, hidden, expert_out.reshape(hidden.shape[0], -1))


def expert_backward(routed, grad_rows, gate_pre, up_pre, hidden, w_gate, w_up, w_down_blocks):
    grad_blocks = grad_rows.reshape(grad_rows.shape[0], w_down_blocks.shape[0], -1)
    grad_hidden = jnp.einsum(
        "sjd,jfd->sf", grad_blocks, w_down_blocks, preferred_element_type=jnp.float32
    )
    logistic = jax.nn.sigmoid(gate_pre)
    activated = gate_pre * logistic
    slope = logistic * (1.0 + gate_pre * (1.0 - logistic))
    grad_gate_pre = (grad_hidden * up_pre * slope).astype(jnp.bfloat16)
    grad_up_pre = (grad_hidden * activated).astype(jnp.bfloat16)
    row_grad = (
        jnp.dot(grad_gate_pre, w_gate.T, preferred_element_type=jnp.float32)
        + jnp.dot(grad_up_pre, w_up.T, preferred_element_type=jnp.float32)
    ).astype(jnp.bfloat16)
    term_gate = jnp.dot(routed.T, grad_gate_pre, preferred_element_type=jnp.float32)
    term_up = jnp.dot(routed.T, grad_up_pre, preferred_element_type=jnp.float32)
    term_down_t = jnp.dot(grad_rows.T, hidden, preferred_element_type=jnp.float32)
    return (row_grad, term_gate, term_up, term_down_t)


def gather_fsdp(shard, n_fsdp):
    copies = jnp.broadcast_to(shard[None], (n_fsdp,) + shard.shape)
    return lax.all_to_all(copies, "fsdp", split_axis=0, concat_axis=0, tiled=True)


def scatter_sum_fsdp(term, n_fsdp):
    me = lax.axis_index("fsdp")
    blocks = term.astype(jnp.bfloat16).reshape((n_fsdp, term.shape[0] // n_fsdp) + term.shape[1:])
    rolled = lax.dynamic_slice_in_dim(jnp.concatenate([blocks, blocks], axis=0), me, n_fsdp, axis=0)
    total = rolled[0].astype(jnp.float32)
    for s in range(1, n_fsdp):
        pairs = [(i, (i + s) % n_fsdp) for i in range(n_fsdp)]
        total = total + lax.ppermute(rolled[s], "fsdp", pairs).astype(jnp.float32)
    return total.astype(jnp.bfloat16)


def per_device(tokens, expert_ids, route_probs, gate_weight, up_weight, down_weight, cotangent):
    n_expert = lax.axis_size("expert")
    n_fsdp = lax.axis_size("fsdp")
    experts = n_expert * gate_weight.shape[0]
    tok_dev, choose = expert_ids.shape
    features = tokens.shape[1]
    capacity = tok_dev * choose * 9 // (experts * 8)
    slot_count = experts * capacity
    dispatch, counts = routing(expert_ids, experts, capacity)
    dispatch_pair = dispatch.astype(jnp.bfloat16)
    dispatch_tok = jnp.sum(dispatch.reshape(slot_count, tok_dev, choose), axis=2).astype(jnp.bfloat16)
    outgoing = jnp.dot(dispatch_tok, tokens, preferred_element_type=jnp.float32).astype(jnp.bfloat16)
    count_rows = jnp.zeros((experts, 1, features), jnp.bfloat16)
    count_rows = count_rows.at[:, 0, 0].set(counts.astype(jnp.bfloat16))
    payload = jnp.concatenate([outgoing.reshape(experts, capacity, features), count_rows], axis=1)
    arrived_all = lax.all_to_all(payload, "expert", split_axis=0, concat_axis=0, tiled=True)
    arrived = arrived_all[:, :capacity]
    arrived_counts = arrived_all[:, capacity, 0:1]
    upstream = cotangent.astype(jnp.float32)
    slot_probs = jnp.sum(
        jnp.where(dispatch, route_probs.reshape(1, tok_dev * choose), 0.0), axis=1
    )
    slot_cot = jnp.dot(dispatch_tok, cotangent, preferred_element_type=jnp.float32)
    outgoing_grad = (slot_probs[:, None] * slot_cot).astype(jnp.bfloat16)
    arrived_all, outgoing_grad = lax.optimization_barrier((arrived_all, outgoing_grad))
    arrived_grad = lax.all_to_all(
        outgoing_grad.reshape(experts, capacity, features), "expert", split_axis=0, concat_axis=0, tiled=True
    )
    routed = arrived.reshape(slot_count, features)
    grad_rows = arrived_grad.reshape(slot_count, features)
    live_mask = jnp.arange(capacity, dtype=jnp.float32)[None, :] < arrived_counts.astype(jnp.float32)
    live_mask = live_mask.astype(jnp.float32).reshape(slot_count)
    w_gate = lax.all_gather(gate_weight, "fsdp", axis=1, tiled=True)[0]
    w_up = lax.all_gather(up_weight, "fsdp", axis=1, tiled=True)[0]
    w_down = lax.all_gather(down_weight, "fsdp", axis=2, tiled=True)[0]
    w_down_blocks = w_down.reshape(w_down.shape[0], n_fsdp, -1).swapaxes(0, 1)
    gate_pre, up_pre, hidden, expert_out = expert_forward(routed, live_mask, w_gate, w_up, w_down_blocks)
    returned = lax.all_to_all(
        expert_out.reshape(n_expert, capacity, features), "expert", split_axis=0, concat_axis=0, tiled=True
    )
    row_grad, term_gate, term_up, term_down_t = expert_backward(
        routed, grad_rows, gate_pre, up_pre, hidden, w_gate, w_up, w_down_blocks
    )
    returned_grad = lax.all_to_all(
        row_grad.reshape(n_expert, capacity, features), "expert", split_axis=0, concat_axis=0, tiled=True
    )
    summed_down = lax.psum_scatter(
        term_down_t.T.astype(jnp.bfloat16), "fsdp", scatter_dimension=1, tiled=True
    )
    summed_down, term_gate = lax.optimization_barrier((summed_down, term_gate))
    summed_gate = lax.psum_scatter(
        term_gate.astype(jnp.bfloat16), "fsdp", scatter_dimension=0, tiled=True
    )
    summed_up = scatter_sum_fsdp(term_up, n_fsdp)
    combined = lax.dot_general(
        dispatch_pair,
        returned.reshape(slot_count, features),
        (((0,), (0,)), ((), ())),
        preferred_element_type=jnp.float32,
    ).reshape(tok_dev, choose, features)
    mixed = jnp.einsum("tk,tkd->td", route_probs, combined).astype(jnp.bfloat16)
    grad_probs = jnp.einsum("td,tkd->tk", upstream, combined)
    grad_tokens = lax.dot_general(
        dispatch_tok,
        returned_grad.reshape(slot_count, features),
        (((0,), (0,)), ((), ())),
        preferred_element_type=jnp.float32,
    ).astype(jnp.bfloat16)
    return (
        mixed,
        grad_probs,
        grad_tokens,
        summed_gate[None],
        summed_up[None],
        summed_down[None],
    )


def solution(mesh):
    return jax.shard_map(
        per_device,
        mesh=mesh,
        in_specs=(
            P(("expert", "fsdp"), None),
            P(("expert", "fsdp"), None),
            P(("expert", "fsdp"), None),
            P("expert", "fsdp", None),
            P("expert", "fsdp", None),
            P("expert", None, "fsdp"),
            P(("expert", "fsdp"), None),
        ),
        out_specs=(
            P(("expert", "fsdp"), None),
            P(("expert", "fsdp"), None),
            P(("expert", "fsdp"), None),
            P("expert", "fsdp", None),
            P("expert", "fsdp", None),
            P("expert", None, "fsdp"),
        ),
        check_vma=False,
    )
```

```python
import jax
import jax.numpy as jnp
from jax import lax
from jax.sharding import PartitionSpec as P


def routing(id_rows, experts, capacity):
    flat_ids = id_rows.reshape(-1)
    onehot = (flat_ids[:, None] == jnp.arange(experts, dtype=jnp.int32)[None, :]).astype(jnp.int32)
    before = jnp.cumsum(onehot, axis=0) - onehot
    slot_index = jnp.sum(before * onehot, axis=1)
    target = flat_ids * capacity + slot_index
    slots = experts * capacity
    dispatch = jnp.arange(slots, dtype=jnp.int32)[:, None] == target[None, :]
    return (dispatch, jnp.sum(onehot, axis=0))


def expert_backward(routed, grad_rows, gate_pre, up_pre, hidden, w_gate, w_up, w_down_blocks):
    grad_blocks = grad_rows.reshape(grad_rows.shape[0], w_down_blocks.shape[0], -1)
    grad_hidden = jnp.einsum(
        "sjd,jfd->sf", grad_blocks, w_down_blocks, preferred_element_type=jnp.float32
    )
    logistic = jax.nn.sigmoid(gate_pre)
    activated = gate_pre * logistic
    slope = logistic * (1.0 + gate_pre * (1.0 - logistic))
    grad_gate_pre = (grad_hidden * up_pre * slope).astype(jnp.bfloat16)
    grad_up_pre = (grad_hidden * activated).astype(jnp.bfloat16)
    row_grad = (
        jnp.dot(grad_gate_pre, w_gate.T, preferred_element_type=jnp.float32)
        + jnp.dot(grad_up_pre, w_up.T, preferred_element_type=jnp.float32)
    ).astype(jnp.bfloat16)
    term_gate = jnp.dot(routed.T, grad_gate_pre, preferred_element_type=jnp.float32)
    term_up = jnp.dot(routed.T, grad_up_pre, preferred_element_type=jnp.float32)
    return (row_grad, term_gate, term_up)


def gather_fsdp(shard, n_fsdp):
    copies = jnp.broadcast_to(shard[None], (n_fsdp,) + shard.shape)
    return lax.all_to_all(copies, "fsdp", split_axis=0, concat_axis=0, tiled=True)


def scatter_sum_fsdp(term, n_fsdp):
    me = lax.axis_index("fsdp")
    blocks = term.astype(jnp.bfloat16).reshape((n_fsdp, term.shape[0] // n_fsdp) + term.shape[1:])
    rolled = lax.dynamic_slice_in_dim(jnp.concatenate([blocks, blocks], axis=0), me, n_fsdp, axis=0)
    total = rolled[0].astype(jnp.float32)
    for s in range(1, n_fsdp):
        pairs = [(i, (i + s) % n_fsdp) for i in range(n_fsdp)]
        total = total + lax.ppermute(rolled[s], "fsdp", pairs).astype(jnp.float32)
    return total.astype(jnp.bfloat16)


def per_device(tokens, expert_ids, route_probs, gate_weight, up_weight, down_weight, cotangent):
    n_expert = lax.axis_size("expert")
    n_fsdp = lax.axis_size("fsdp")
    experts = n_expert * gate_weight.shape[0]
    tok_dev, choose = expert_ids.shape
    features = tokens.shape[1]
    capacity = tok_dev * choose * 9 // (experts * 8)
    slot_count = experts * capacity
    dispatch, counts = routing(expert_ids, experts, capacity)
    dispatch_pair = dispatch.astype(jnp.bfloat16)
    dispatch_tok = jnp.sum(dispatch.reshape(slot_count, tok_dev, choose), axis=2).astype(jnp.bfloat16)
    outgoing = jnp.dot(dispatch_tok, tokens, preferred_element_type=jnp.float32).astype(jnp.bfloat16)
    count_rows = jnp.zeros((experts, 1, features), jnp.bfloat16)
    count_rows = count_rows.at[:, 0, 0].set(counts.astype(jnp.bfloat16))
    payload = jnp.concatenate([outgoing.reshape(experts, capacity, features), count_rows], axis=1)
    arrived_all = lax.all_to_all(payload, "expert", split_axis=0, concat_axis=0, tiled=True)
    arrived = arrived_all[:, :capacity]
    arrived_counts = arrived_all[:, capacity, 0:1]
    upstream = cotangent.astype(jnp.float32)
    slot_probs = jnp.sum(
        jnp.where(dispatch, route_probs.reshape(1, tok_dev * choose), 0.0), axis=1
    )
    slot_cot = jnp.dot(dispatch_tok, cotangent, preferred_element_type=jnp.float32)
    outgoing_grad = (slot_probs[:, None] * slot_cot).astype(jnp.bfloat16)
    arrived_all, outgoing_grad = lax.optimization_barrier((arrived_all, outgoing_grad))
    arrived_grad = lax.all_to_all(
        outgoing_grad.reshape(experts, capacity, features), "expert", split_axis=0, concat_axis=0, tiled=True
    )
    routed = arrived.reshape(slot_count, features)
    grad_rows = arrived_grad.reshape(slot_count, features)
    live_mask = jnp.arange(capacity, dtype=jnp.float32)[None, :] < arrived_counts.astype(jnp.float32)
    live_mask = live_mask.astype(jnp.float32).reshape(slot_count)
    w_gate = lax.all_gather(gate_weight, "fsdp", axis=1, tiled=True)[0]
    w_up = lax.all_gather(up_weight, "fsdp", axis=1, tiled=True)[0]
    w_down = lax.all_gather(down_weight, "fsdp", axis=2, tiled=True)[0]
    w_down_blocks = w_down.reshape(w_down.shape[0], n_fsdp, -1).swapaxes(0, 1)
    gate_pre = jnp.dot(routed, w_gate, preferred_element_type=jnp.float32)
    up_pre = jnp.dot(routed, w_up, preferred_element_type=jnp.float32)
    hidden = (jax.nn.silu(gate_pre) * up_pre * live_mask[:, None]).astype(jnp.bfloat16)
    term_down_t = jnp.dot(grad_rows.T, hidden, preferred_element_type=jnp.float32)
    term_down_t, w_down_blocks = lax.optimization_barrier((term_down_t, w_down_blocks))
    summed_down = lax.psum_scatter(
        term_down_t.T.astype(jnp.bfloat16), "fsdp", scatter_dimension=1, tiled=True
    )
    expert_out = jnp.einsum(
        "sf,jfd->sjd", hidden, w_down_blocks, preferred_element_type=jnp.float32
    ).astype(jnp.bfloat16).reshape(slot_count, features)
    returned = lax.all_to_all(
        expert_out.reshape(n_expert, capacity, features), "expert", split_axis=0, concat_axis=0, tiled=True
    )
    row_grad, term_gate, term_up = expert_backward(
        routed, grad_rows, gate_pre, up_pre, hidden, w_gate, w_up, w_down_blocks
    )
    returned_grad = lax.all_to_all(
        row_grad.reshape(n_expert, capacity, features), "expert", split_axis=0, concat_axis=0, tiled=True
    )
    summed_down, term_gate = lax.optimization_barrier((summed_down, term_gate))
    summed_gate = lax.psum_scatter(
        term_gate.astype(jnp.bfloat16), "fsdp", scatter_dimension=0, tiled=True
    )
    summed_up = scatter_sum_fsdp(term_up, n_fsdp)
    combined = lax.dot_general(
        dispatch_pair,
        returned.reshape(slot_count, features),
        (((0,), (0,)), ((), ())),
        preferred_element_type=jnp.float32,
    ).reshape(tok_dev, choose, features)
    mixed = jnp.einsum("tk,tkd->td", route_probs, combined).astype(jnp.bfloat16)
    grad_probs = jnp.einsum("td,tkd->tk", upstream, combined)
    grad_tokens = lax.dot_general(
        dispatch_tok,
        returned_grad.reshape(slot_count, features),
        (((0,), (0,)), ((), ())),
        preferred_element_type=jnp.float32,
    ).astype(jnp.bfloat16)
    return (
        mixed,
        grad_probs,
        grad_tokens,
        summed_gate[None],
        summed_up[None],
        summed_down[None],
    )


def solution(mesh):
    return jax.shard_map(
        per_device,
        mesh=mesh,
        in_specs=(
            P(("expert", "fsdp"), None),
            P(("expert", "fsdp"), None),
            P(("expert", "fsdp"), None),
            P("expert", "fsdp", None),
            P("expert", "fsdp", None),
            P("expert", None, "fsdp"),
            P(("expert", "fsdp"), None),
        ),
        out_specs=(
            P(("expert", "fsdp"), None),
            P(("expert", "fsdp"), None),
            P(("expert", "fsdp"), None),
            P("expert", "fsdp", None),
            P("expert", "fsdp", None),
            P("expert", None, "fsdp"),
        ),
        check_vma=False,
    )
```

```python
import jax
import jax.numpy as jnp
from jax import lax
from jax.sharding import PartitionSpec as P


def routing(id_rows, experts, capacity):
    flat_ids = id_rows.reshape(-1)
    onehot = (flat_ids[:, None] == jnp.arange(experts, dtype=jnp.int32)[None, :]).astype(jnp.int32)
    before = jnp.cumsum(onehot, axis=0) - onehot
    slot_index = jnp.sum(before * onehot, axis=1)
    target = flat_ids * capacity + slot_index
    slots = experts * capacity
    dispatch = jnp.arange(slots, dtype=jnp.int32)[:, None] == target[None, :]
    return (dispatch, jnp.sum(onehot, axis=0))


def expert_backward(routed, grad_rows, gate_pre, up_pre, hidden, w_gate, w_up, w_down_blocks):
    grad_blocks = grad_rows.reshape(grad_rows.shape[0], w_down_blocks.shape[0], -1)
    grad_hidden = jnp.einsum(
        "sjd,jfd->sf", grad_blocks, w_down_blocks, preferred_element_type=jnp.float32
    )
    logistic = jax.nn.sigmoid(gate_pre)
    activated = gate_pre * logistic
    slope = logistic * (1.0 + gate_pre * (1.0 - logistic))
    grad_gate_pre = (grad_hidden * up_pre * slope).astype(jnp.bfloat16)
    grad_up_pre = (grad_hidden * activated).astype(jnp.bfloat16)
    row_grad = (
        jnp.dot(grad_gate_pre, w_gate.T, preferred_element_type=jnp.float32)
        + jnp.dot(grad_up_pre, w_up.T, preferred_element_type=jnp.float32)
    ).astype(jnp.bfloat16)
    term_gate = jnp.dot(routed.T, grad_gate_pre, preferred_element_type=jnp.float32)
    term_up = jnp.dot(routed.T, grad_up_pre, preferred_element_type=jnp.float32)
    return (row_grad, term_gate, term_up)


def gather_fsdp(shard, n_fsdp):
    me = lax.axis_index("fsdp")
    got = [shard]
    for s in range(1, n_fsdp):
        pairs = [(i, (i + s) % n_fsdp) for i in range(n_fsdp)]
        got.append(lax.ppermute(shard, "fsdp", pairs))
    ring = jnp.stack(got[::-1], axis=0)
    doubled = jnp.concatenate([ring, ring], axis=0)
    return lax.dynamic_slice_in_dim(doubled, (n_fsdp - 1 - me) % n_fsdp, n_fsdp, axis=0)


def scatter_sum_fsdp(term, n_fsdp):
    me = lax.axis_index("fsdp")
    blocks = term.astype(jnp.bfloat16).reshape((n_fsdp, term.shape[0] // n_fsdp) + term.shape[1:])
    rolled = lax.dynamic_slice_in_dim(jnp.concatenate([blocks, blocks], axis=0), me, n_fsdp, axis=0)
    total = rolled[0].astype(jnp.float32)
    for s in range(1, n_fsdp):
        pairs = [(i, (i + s) % n_fsdp) for i in range(n_fsdp)]
        total = total + lax.ppermute(rolled[s], "fsdp", pairs).astype(jnp.float32)
    return total.astype(jnp.bfloat16)


def per_device(tokens, expert_ids, route_probs, gate_weight, up_weight, down_weight, cotangent):
    n_expert = lax.axis_size("expert")
    n_fsdp = lax.axis_size("fsdp")
    experts = n_expert * gate_weight.shape[0]
    tok_dev, choose = expert_ids.shape
    features = tokens.shape[1]
    capacity = tok_dev * choose * 9 // (experts * 8)
    slot_count = experts * capacity
    dispatch, counts = routing(expert_ids, experts, capacity)
    dispatch_pair = dispatch.astype(jnp.bfloat16)
    dispatch_tok = jnp.sum(dispatch.reshape(slot_count, tok_dev, choose), axis=2).astype(jnp.bfloat16)
    outgoing = jnp.dot(dispatch_tok, tokens, preferred_element_type=jnp.float32).astype(jnp.bfloat16)
    count_rows = jnp.zeros((experts, 1, features), jnp.bfloat16)
    count_rows = count_rows.at[:, 0, 0].set(counts.astype(jnp.bfloat16))
    payload = jnp.concatenate([outgoing.reshape(experts, capacity, features), count_rows], axis=1)
    arrived_all = lax.all_to_all(payload, "expert", split_axis=0, concat_axis=0, tiled=True)
    arrived = arrived_all[:, :capacity]
    arrived_counts = arrived_all[:, capacity, 0:1]
    upstream = cotangent.astype(jnp.float32)
    slot_probs = jnp.sum(
        jnp.where(dispatch, route_probs.reshape(1, tok_dev * choose), 0.0), axis=1
    )
    slot_cot = jnp.dot(dispatch_tok, cotangent, preferred_element_type=jnp.float32)
    outgoing_grad = (slot_probs[:, None] * slot_cot).astype(jnp.bfloat16)
    arrived_all, outgoing_grad = lax.optimization_barrier((arrived_all, outgoing_grad))
    arrived_grad = lax.all_to_all(
        outgoing_grad.reshape(experts, capacity, features), "expert", split_axis=0, concat_axis=0, tiled=True
    )
    routed = arrived.reshape(slot_count, features)
    grad_rows = arrived_grad.reshape(slot_count, features)
    live_mask = jnp.arange(capacity, dtype=jnp.float32)[None, :] < arrived_counts.astype(jnp.float32)
    live_mask = live_mask.astype(jnp.float32).reshape(slot_count)
    w_gate = gather_fsdp(gate_weight[0], n_fsdp).reshape(features, -1)
    w_up = lax.all_gather(up_weight, "fsdp", axis=1, tiled=True)[0]
    w_down = lax.all_gather(down_weight, "fsdp", axis=2, tiled=True)[0]
    w_down_blocks = w_down.reshape(w_down.shape[0], n_fsdp, -1).swapaxes(0, 1)
    gate_pre = jnp.dot(routed, w_gate, preferred_element_type=jnp.float32)
    up_pre = jnp.dot(routed, w_up, preferred_element_type=jnp.float32)
    hidden = (jax.nn.silu(gate_pre) * up_pre * live_mask[:, None]).astype(jnp.bfloat16)
    term_down_t = jnp.dot(grad_rows.T, hidden, preferred_element_type=jnp.float32)
    term_down_t, w_down_blocks = lax.optimization_barrier((term_down_t, w_down_blocks))
    summed_down = lax.psum_scatter(
        term_down_t.T.astype(jnp.bfloat16), "fsdp", scatter_dimension=1, tiled=True
    )
    expert_out = jnp.einsum(
        "sf,jfd->sjd", hidden, w_down_blocks, preferred_element_type=jnp.float32
    ).astype(jnp.bfloat16).reshape(slot_count, features)
    returned = lax.all_to_all(
        expert_out.reshape(n_expert, capacity, features), "expert", split_axis=0, concat_axis=0, tiled=True
    )
    row_grad, term_gate, term_up = expert_backward(
        routed, grad_rows, gate_pre, up_pre, hidden, w_gate, w_up, w_down_blocks
    )
    returned_grad = lax.all_to_all(
        row_grad.reshape(n_expert, capacity, features), "expert", split_axis=0, concat_axis=0, tiled=True
    )
    summed_gate = lax.psum_scatter(
        term_gate.astype(jnp.bfloat16), "fsdp", scatter_dimension=0, tiled=True
    )
    summed_up = scatter_sum_fsdp(term_up, n_fsdp)
    combined = lax.dot_general(
        dispatch_pair,
        returned.reshape(slot_count, features),
        (((0,), (0,)), ((), ())),
        preferred_element_type=jnp.float32,
    ).reshape(tok_dev, choose, features)
    mixed = jnp.einsum("tk,tkd->td", route_probs, combined).astype(jnp.bfloat16)
    grad_probs = jnp.einsum("td,tkd->tk", upstream, combined)
    grad_tokens = lax.dot_general(
        dispatch_tok,
        returned_grad.reshape(slot_count, features),
        (((0,), (0,)), ((), ())),
        preferred_element_type=jnp.float32,
    ).astype(jnp.bfloat16)
    return (
        mixed,
        grad_probs,
        grad_tokens,
        summed_gate[None],
        summed_up[None],
        summed_down[None],
    )


def solution(mesh):
    return jax.shard_map(
        per_device,
        mesh=mesh,
        in_specs=(
            P(("expert", "fsdp"), None),
            P(("expert", "fsdp"), None),
            P(("expert", "fsdp"), None),
            P("expert", "fsdp", None),
            P("expert", "fsdp", None),
            P("expert", None, "fsdp"),
            P(("expert", "fsdp"), None),
        ),
        out_specs=(
            P(("expert", "fsdp"), None),
            P(("expert", "fsdp"), None),
            P(("expert", "fsdp"), None),
            P("expert", "fsdp", None),
            P("expert", "fsdp", None),
            P("expert", None, "fsdp"),
        ),
        check_vma=False,
    )
```

```python
import jax
import jax.numpy as jnp
from jax import lax
from jax.sharding import PartitionSpec as P


def routing(id_rows, experts, capacity):
    flat_ids = id_rows.reshape(-1)
    onehot = (flat_ids[:, None] == jnp.arange(experts, dtype=jnp.int32)[None, :]).astype(jnp.int32)
    before = jnp.cumsum(onehot, axis=0) - onehot
    slot_index = jnp.sum(before * onehot, axis=1)
    target = flat_ids * capacity + slot_index
    slots = experts * capacity
    dispatch = jnp.arange(slots, dtype=jnp.int32)[:, None] == target[None, :]
    return (dispatch, jnp.sum(onehot, axis=0))


def expert_backward(routed, grad_rows, gate_pre, up_pre, hidden, w_gate, w_up, w_down_blocks):
    grad_blocks = grad_rows.reshape(grad_rows.shape[0], w_down_blocks.shape[0], -1)
    grad_hidden = jnp.einsum(
        "sjd,jfd->sf", grad_blocks, w_down_blocks, preferred_element_type=jnp.float32
    )
    logistic = jax.nn.sigmoid(gate_pre)
    activated = gate_pre * logistic
    slope = logistic * (1.0 + gate_pre * (1.0 - logistic))
    grad_gate_pre = (grad_hidden * up_pre * slope).astype(jnp.bfloat16)
    grad_up_pre = (grad_hidden * activated).astype(jnp.bfloat16)
    row_grad = (
        jnp.dot(grad_gate_pre, w_gate.T, preferred_element_type=jnp.float32)
        + jnp.dot(grad_up_pre, w_up.T, preferred_element_type=jnp.float32)
    ).astype(jnp.bfloat16)
    term_gate = jnp.dot(routed.T, grad_gate_pre, preferred_element_type=jnp.float32)
    term_up = jnp.dot(routed.T, grad_up_pre, preferred_element_type=jnp.float32)
    return (row_grad, term_gate, term_up)


def gather_fsdp(shard, n_fsdp):
    copies = jnp.broadcast_to(shard[None], (n_fsdp,) + shard.shape)
    return lax.all_to_all(copies, "fsdp", split_axis=0, concat_axis=0, tiled=True)


def scatter_sum_fsdp(term, n_fsdp):
    me = lax.axis_index("fsdp")
    blocks = term.astype(jnp.bfloat16).reshape((n_fsdp, term.shape[0] // n_fsdp) + term.shape[1:])
    rolled = lax.dynamic_slice_in_dim(jnp.concatenate([blocks, blocks], axis=0), me, n_fsdp, axis=0)
    total = rolled[0].astype(jnp.float32)
    for s in range(1, n_fsdp):
        pairs = [(i, (i + s) % n_fsdp) for i in range(n_fsdp)]
        total = total + lax.ppermute(rolled[s], "fsdp", pairs).astype(jnp.float32)
    return total.astype(jnp.bfloat16)


def per_device(tokens, expert_ids, route_probs, gate_weight, up_weight, down_weight, cotangent):
    n_expert = lax.axis_size("expert")
    n_fsdp = lax.axis_size("fsdp")
    experts = n_expert * gate_weight.shape[0]
    tok_dev, choose = expert_ids.shape
    features = tokens.shape[1]
    capacity = tok_dev * choose * 9 // (experts * 8)
    slot_count = experts * capacity
    dispatch, counts = routing(expert_ids, experts, capacity)
    dispatch_pair = dispatch.astype(jnp.bfloat16)
    dispatch_tok = jnp.sum(dispatch.reshape(slot_count, tok_dev, choose), axis=2).astype(jnp.bfloat16)
    outgoing = jnp.dot(dispatch_tok, tokens, preferred_element_type=jnp.float32).astype(jnp.bfloat16)
    count_rows = jnp.zeros((experts, 1, features), jnp.bfloat16)
    count_rows = count_rows.at[:, 0, 0].set(counts.astype(jnp.bfloat16))
    payload = jnp.concatenate([outgoing.reshape(experts, capacity, features), count_rows], axis=1)
    arrived_all = lax.all_to_all(payload, "expert", split_axis=0, concat_axis=0, tiled=True)
    arrived = arrived_all[:, :capacity]
    arrived_counts = arrived_all[:, capacity, 0:1]
    upstream = cotangent.astype(jnp.float32)
    slot_probs = jnp.sum(
        jnp.where(dispatch, route_probs.reshape(1, tok_dev * choose), 0.0), axis=1
    )
    slot_cot = jnp.dot(dispatch_tok, cotangent, preferred_element_type=jnp.float32)
    outgoing_grad = (slot_probs[:, None] * slot_cot).astype(jnp.bfloat16)
    arrived_all, outgoing_grad = lax.optimization_barrier((arrived_all, outgoing_grad))
    arrived_grad = lax.all_to_all(
        outgoing_grad.reshape(experts, capacity, features), "expert", split_axis=0, concat_axis=0, tiled=True
    )
    routed = arrived.reshape(slot_count, features)
    grad_rows = arrived_grad.reshape(slot_count, features)
    live_mask = jnp.arange(capacity, dtype=jnp.float32)[None, :] < arrived_counts.astype(jnp.float32)
    live_mask = live_mask.astype(jnp.float32).reshape(slot_count)
    w_gate = lax.all_gather(gate_weight, "fsdp", axis=1, tiled=True)[0]
    w_up = lax.all_gather(up_weight, "fsdp", axis=1, tiled=True)[0]
    w_down = lax.all_gather(down_weight, "fsdp", axis=2, tiled=True)[0]
    w_down_blocks = w_down.reshape(w_down.shape[0], n_fsdp, -1).swapaxes(0, 1)
    gate_pre = jnp.dot(routed, w_gate, preferred_element_type=jnp.float32)
    up_pre = jnp.dot(routed, w_up, preferred_element_type=jnp.float32)
    hidden = (jax.nn.silu(gate_pre) * up_pre * live_mask[:, None]).astype(jnp.bfloat16)
    term_down_t = jnp.dot(grad_rows.T, hidden, preferred_element_type=jnp.float32)
    term_down_t, w_down_blocks = lax.optimization_barrier((term_down_t, w_down_blocks))
    summed_down = lax.psum_scatter(
        term_down_t.T.astype(jnp.bfloat16), "fsdp", scatter_dimension=1, tiled=True
    )
    expert_out = jnp.einsum(
        "sf,jfd->sjd", hidden, w_down_blocks, preferred_element_type=jnp.float32
    ).astype(jnp.bfloat16).reshape(slot_count, features)
    returned = lax.all_to_all(
        expert_out.reshape(n_expert, capacity, features), "expert", split_axis=0, concat_axis=0, tiled=True
    )
    row_grad, term_gate, term_up = expert_backward(
        routed, grad_rows, gate_pre, up_pre, hidden, w_gate, w_up, w_down_blocks
    )
    returned_grad = lax.all_to_all(
        row_grad.reshape(n_expert, capacity, features), "expert", split_axis=0, concat_axis=0, tiled=True
    )
    summed_gate = lax.psum_scatter(
        term_gate.astype(jnp.bfloat16), "fsdp", scatter_dimension=0, tiled=True
    )
    summed_up = scatter_sum_fsdp(term_up, n_fsdp)
    combined = lax.dot_general(
        dispatch_pair,
        returned.reshape(slot_count, features),
        (((0,), (0,)), ((), ())),
        preferred_element_type=jnp.float32,
    ).reshape(tok_dev, choose, features)
    mixed = jnp.einsum("tk,tkd->td", route_probs, combined).astype(jnp.bfloat16)
    grad_probs = jnp.einsum("td,tkd->tk", upstream, combined)
    grad_tokens = lax.dot_general(
        dispatch_tok,
        returned_grad.reshape(slot_count, features),
        (((0,), (0,)), ((), ())),
        preferred_element_type=jnp.float32,
    ).astype(jnp.bfloat16)
    return (
        mixed,
        grad_probs,
        grad_tokens,
        summed_gate[None],
        summed_up[None],
        summed_down[None],
    )


def solution(mesh):
    return jax.shard_map(
        per_device,
        mesh=mesh,
        in_specs=(
            P(("expert", "fsdp"), None),
            P(("expert", "fsdp"), None),
            P(("expert", "fsdp"), None),
            P("expert", "fsdp", None),
            P("expert", "fsdp", None),
            P("expert", None, "fsdp"),
            P(("expert", "fsdp"), None),
        ),
        out_specs=(
            P(("expert", "fsdp"), None),
            P(("expert", "fsdp"), None),
            P(("expert", "fsdp"), None),
            P("expert", "fsdp", None),
            P("expert", "fsdp", None),
            P("expert", None, "fsdp"),
        ),
        check_vma=False,
    )
```

```python
import jax
import jax.numpy as jnp
from jax import lax
from jax.sharding import PartitionSpec as P


def routing(id_rows, experts, capacity):
    flat_ids = id_rows.reshape(-1)
    onehot = (flat_ids[:, None] == jnp.arange(experts, dtype=jnp.int32)[None, :]).astype(jnp.int32)
    before = jnp.cumsum(onehot, axis=0) - onehot
    slot_index = jnp.sum(before * onehot, axis=1)
    target = flat_ids * capacity + slot_index
    slots = experts * capacity
    dispatch = jnp.arange(slots, dtype=jnp.int32)[:, None] == target[None, :]
    return (dispatch, jnp.sum(onehot, axis=0))


def expert_backward(routed, grad_rows, gate_pre, up_pre, hidden, w_gate, w_up, w_down_blocks):
    grad_blocks = grad_rows.reshape(grad_rows.shape[0], w_down_blocks.shape[0], -1)
    grad_hidden = jnp.einsum(
        "sjd,jfd->sf", grad_blocks, w_down_blocks, preferred_element_type=jnp.float32
    )
    logistic = jax.nn.sigmoid(gate_pre)
    activated = gate_pre * logistic
    slope = logistic * (1.0 + gate_pre * (1.0 - logistic))
    grad_gate_pre = (grad_hidden * up_pre * slope).astype(jnp.bfloat16)
    grad_up_pre = (grad_hidden * activated).astype(jnp.bfloat16)
    row_grad = (
        jnp.dot(grad_gate_pre, w_gate.T, preferred_element_type=jnp.float32)
        + jnp.dot(grad_up_pre, w_up.T, preferred_element_type=jnp.float32)
    ).astype(jnp.bfloat16)
    term_gate = jnp.dot(routed.T, grad_gate_pre, preferred_element_type=jnp.float32)
    term_up = jnp.dot(routed.T, grad_up_pre, preferred_element_type=jnp.float32)
    return (row_grad, term_gate, term_up)


def gather_fsdp(shard, n_fsdp):
    copies = jnp.broadcast_to(shard[None], (n_fsdp,) + shard.shape)
    return lax.all_to_all(copies, "fsdp", split_axis=0, concat_axis=0, tiled=True)


def scatter_sum_fsdp(term, n_fsdp):
    me = lax.axis_index("fsdp")
    blocks = term.astype(jnp.bfloat16).reshape((n_fsdp, term.shape[0] // n_fsdp) + term.shape[1:])
    rolled = lax.dynamic_slice_in_dim(jnp.concatenate([blocks, blocks], axis=0), me, n_fsdp, axis=0)
    total = rolled[0].astype(jnp.float32)
    for s in range(1, n_fsdp):
        pairs = [(i, (i + s) % n_fsdp) for i in range(n_fsdp)]
        total = total + lax.ppermute(rolled[s], "fsdp", pairs).astype(jnp.float32)
    return total.astype(jnp.bfloat16)


def per_device(tokens, expert_ids, route_probs, gate_weight, up_weight, down_weight, cotangent):
    n_expert = lax.axis_size("expert")
    n_fsdp = lax.axis_size("fsdp")
    experts = n_expert * gate_weight.shape[0]
    tok_dev, choose = expert_ids.shape
    features = tokens.shape[1]
    capacity = tok_dev * choose * 9 // (experts * 8)
    slot_count = experts * capacity
    dispatch, counts = routing(expert_ids, experts, capacity)
    dispatch_pair = dispatch.astype(jnp.bfloat16)
    dispatch_tok = jnp.sum(dispatch.reshape(slot_count, tok_dev, choose), axis=2).astype(jnp.bfloat16)
    block = capacity + 1
    block_tok = jnp.concatenate(
        [dispatch_tok.reshape(experts, capacity, tok_dev), jnp.zeros((experts, 1, tok_dev), jnp.bfloat16)],
        axis=1,
    ).reshape(experts * block, tok_dev)
    spread = jnp.dot(block_tok, tokens, preferred_element_type=jnp.float32).reshape(experts, block, features)
    row_at = jnp.arange(block, dtype=jnp.int32)[None, :, None]
    col_at = jnp.arange(features, dtype=jnp.int32)[None, None, :]
    count_at = (row_at == capacity) & (col_at == 0)
    payload = jnp.where(count_at, counts.astype(jnp.float32)[:, None, None], spread).astype(jnp.bfloat16)
    arrived_all = lax.all_to_all(payload, "expert", split_axis=0, concat_axis=0, tiled=True)
    arrived = arrived_all[:, :capacity]
    arrived_counts = arrived_all[:, capacity, 0:1]
    upstream = cotangent.astype(jnp.float32)
    slot_probs = jnp.sum(
        jnp.where(dispatch, route_probs.reshape(1, tok_dev * choose), 0.0), axis=1
    )
    slot_cot = jnp.dot(dispatch_tok, cotangent, preferred_element_type=jnp.float32)
    outgoing_grad = (slot_probs[:, None] * slot_cot).astype(jnp.bfloat16)
    arrived_all, outgoing_grad = lax.optimization_barrier((arrived_all, outgoing_grad))
    arrived_grad = lax.all_to_all(
        outgoing_grad.reshape(experts, capacity, features), "expert", split_axis=0, concat_axis=0, tiled=True
    )
    routed = arrived.reshape(slot_count, features)
    grad_rows = arrived_grad.reshape(slot_count, features)
    live_mask = jnp.arange(capacity, dtype=jnp.float32)[None, :] < arrived_counts.astype(jnp.float32)
    live_mask = live_mask.astype(jnp.float32).reshape(slot_count)
    w_gate = lax.all_gather(gate_weight, "fsdp", axis=1, tiled=True)[0]
    w_up = lax.all_gather(up_weight, "fsdp", axis=1, tiled=True)[0]
    w_down = lax.all_gather(down_weight, "fsdp", axis=2, tiled=True)[0]
    w_down_blocks = w_down.reshape(w_down.shape[0], n_fsdp, -1).swapaxes(0, 1)
    gate_pre = jnp.dot(routed, w_gate, preferred_element_type=jnp.float32)
    up_pre = jnp.dot(routed, w_up, preferred_element_type=jnp.float32)
    hidden = (jax.nn.silu(gate_pre) * up_pre * live_mask[:, None]).astype(jnp.bfloat16)
    term_down_t = jnp.dot(grad_rows.T, hidden, preferred_element_type=jnp.float32)
    term_down_t, w_down_blocks = lax.optimization_barrier((term_down_t, w_down_blocks))
    summed_down = lax.psum_scatter(
        term_down_t.T.astype(jnp.bfloat16), "fsdp", scatter_dimension=1, tiled=True
    )
    expert_out = jnp.einsum(
        "sf,jfd->sjd", hidden, w_down_blocks, preferred_element_type=jnp.float32
    ).astype(jnp.bfloat16).reshape(slot_count, features)
    returned = lax.all_to_all(
        expert_out.reshape(n_expert, capacity, features), "expert", split_axis=0, concat_axis=0, tiled=True
    )
    row_grad, term_gate, term_up = expert_backward(
        routed, grad_rows, gate_pre, up_pre, hidden, w_gate, w_up, w_down_blocks
    )
    returned_grad = lax.all_to_all(
        row_grad.reshape(n_expert, capacity, features), "expert", split_axis=0, concat_axis=0, tiled=True
    )
    summed_gate = lax.psum_scatter(
        term_gate.astype(jnp.bfloat16), "fsdp", scatter_dimension=0, tiled=True
    )
    summed_up = scatter_sum_fsdp(term_up, n_fsdp)
    combined = lax.dot_general(
        dispatch_pair,
        returned.reshape(slot_count, features),
        (((0,), (0,)), ((), ())),
        preferred_element_type=jnp.float32,
    ).reshape(tok_dev, choose, features)
    mixed = jnp.einsum("tk,tkd->td", route_probs, combined).astype(jnp.bfloat16)
    grad_probs = jnp.einsum("td,tkd->tk", upstream, combined)
    grad_tokens = lax.dot_general(
        dispatch_tok,
        returned_grad.reshape(slot_count, features),
        (((0,), (0,)), ((), ())),
        preferred_element_type=jnp.float32,
    ).astype(jnp.bfloat16)
    return (
        mixed,
        grad_probs,
        grad_tokens,
        summed_gate[None],
        summed_up[None],
        summed_down[None],
    )


def solution(mesh):
    return jax.shard_map(
        per_device,
        mesh=mesh,
        in_specs=(
            P(("expert", "fsdp"), None),
            P(("expert", "fsdp"), None),
            P(("expert", "fsdp"), None),
            P("expert", "fsdp", None),
            P("expert", "fsdp", None),
            P("expert", None, "fsdp"),
            P(("expert", "fsdp"), None),
        ),
        out_specs=(
            P(("expert", "fsdp"), None),
            P(("expert", "fsdp"), None),
            P(("expert", "fsdp"), None),
            P("expert", "fsdp", None),
            P("expert", "fsdp", None),
            P("expert", None, "fsdp"),
        ),
        check_vma=False,
    )
```
